512 devices in a mesh: pipe: 16 (over z_hi, x, core), tensor: 32 (over z_lo, y).
Axes of the slice: x: 4, y: 4, z: 16 (z_hi: 2, z_lo: 8; z = z_hi * 8 + z_lo), core: 2. Of those that a mesh axis runs over, the one named last changes fastest.
Arguments:
- tokens: bfloat16 [512, 8192], P(None, 'pipe'), may hold values from -6 to 6
- out_grad: bfloat16 [512, 8192], P(None, 'pipe'), may hold values from -6 to 6
- w_gate: bfloat16 [8192, 16384], P('pipe', 'tensor'), may hold values from -0.0625 to 0.0625
- w_up: bfloat16 [8192, 16384], P('pipe', 'tensor'), may hold values from -0.0625 to 0.0625
- w_down: bfloat16 [16384, 8192], P('tensor', 'pipe'), may hold values from -0.046875 to 0.046875
Outputs:
- input_grad: float32 [512, 8192], P('tensor', 'pipe')
- gate_mantissa: bfloat16 [8192, 16384], P('pipe', 'tensor')
- gate_scales: float32 [256, 8192], P('pipe', 'tensor')
- up_mantissa: bfloat16 [8192, 16384], P('pipe', 'tensor')
- up_scales: float32 [256, 8192], P('pipe', 'tensor')
- down_mantissa: bfloat16 [16384, 8192], P('tensor', 'pipe')
- down_scales: float32 [8192, 256], P('tensor', 'pipe')
The draws below stay inside these ranges and needn't reach their ends.
All inputs are finite; a program needn't handle non-finite values.
Results may differ from the reference program's by a relative error of at most 0.0049.
Values may be sent and summed in bfloat16 or wider, within the bound.
No kernel may reach another device: no remote copies, remote signals or barrier semaphores. Data moves between devices by JAX's collectives and lax.ppermute only.
A program may use at most 64 MiB of HBM per device.

```python
import jax
import jax.numpy as jnp

D = 8192
HID = 16384
TOKENS = 512


def level_of(key, shape, shards, low, top_value):
    def one(axis_at, shards_of):
        heights = jax.random.uniform(jax.random.fold_in(jax.random.fold_in(key, 6), axis_at), (shards_of,), jnp.float32, low / len(shards), top_value / len(shards))
        return jnp.repeat(jnp.exp(heights), shape[axis_at] // shards_of).reshape((-1,) + (1,) * (len(shape) - axis_at - 1))

    loudness = one(*shards[0])
    for cut in shards[1:]:
        loudness = loudness * one(*cut)
    return loudness


def gaussian(key, shape, deviation, limit, cuts=(), kind=jnp.bfloat16):
    result = deviation * jax.random.normal(key, shape, jnp.float32)
    if cuts:
        result = result * level_of(key, shape, cuts, -0.22, 0.18)
    return jnp.clip(result, -limit, limit).astype(kind)


def setup_inputs(seed: int = 0) -> dict:
    splits = jax.random.split(jax.random.key(seed), 6)
    tokens = gaussian(splits[0], (TOKENS, D), 1.0, 6.0, ((1, 16),))
    out_grad = gaussian(splits[1], (TOKENS, D), 1.0, 6.0, ((1, 16),))
    w_gate = gaussian(splits[2], (D, HID), D ** -0.5, 0.0625, ((0, 16), (1, 32)))
    w_up = gaussian(splits[3], (D, HID), D ** -0.5, 0.0625, ((0, 16), (1, 32)))
    w_down = gaussian(splits[4], (HID, D), HID ** -0.5, 0.046875, ((0, 32), (1, 16)))
    return {"tokens": tokens, "out_grad": out_grad, "w_gate": w_gate, "w_up": w_up, "w_down": w_down}


def quantize_features(grad):
    mags = jnp.abs(grad)
    paired = jnp.maximum(mags[:, 0::2], mags[:, 1::2])
    scales = jnp.max(paired.reshape(paired.shape[0] // 32, 32, paired.shape[1]), axis=1) + 1e-6
    spread = jnp.repeat(scales, 2, axis=1)
    mantissa = (grad.reshape(grad.shape[0] // 32, 32, grad.shape[1]) / spread[:, None, :]).reshape(grad.shape)
    return mantissa.astype(jnp.bfloat16), scales


def quantize_hidden(grad):
    mags = jnp.abs(grad)
    paired = jnp.maximum(mags[0::2], mags[1::2])
    scales = jnp.max(paired.reshape(paired.shape[0], paired.shape[1] // 32, 32), axis=2) + 1e-6
    spread = jnp.repeat(scales, 32, axis=1)
    mantissa = (grad.reshape(grad.shape[0] // 2, 2, grad.shape[1]) / spread[:, None, :]).reshape(grad.shape)
    return mantissa.astype(jnp.bfloat16), scales


def reference(tokens, out_grad, w_gate, w_up, w_down):
    gate = jnp.dot(tokens, w_gate, preferred_element_type=jnp.float32)
    up = jnp.dot(tokens, w_up, preferred_element_type=jnp.float32)
    hidden_grad = jnp.dot(out_grad, w_down.T, preferred_element_type=jnp.float32)
    sigmoid_gate = jax.nn.sigmoid(gate)
    silu_gate = gate * sigmoid_gate
    hidden = (silu_gate * up).astype(jnp.bfloat16)
    gate_grad = (hidden_grad * up * sigmoid_gate * (1.0 + gate * (1.0 - sigmoid_gate))).astype(jnp.bfloat16)
    up_grad = (hidden_grad * silu_gate).astype(jnp.bfloat16)
    input_grad = (jnp.dot(gate_grad, w_gate.T, preferred_element_type=jnp.float32)
                  + jnp.dot(up_grad, w_up.T, preferred_element_type=jnp.float32))
    gate_mantissa, gate_scales = quantize_features(jnp.dot(tokens.T, gate_grad, preferred_element_type=jnp.float32))
    up_mantissa, up_scales = quantize_features(jnp.dot(tokens.T, up_grad, preferred_element_type=jnp.float32))
    down_mantissa, down_scales = quantize_hidden(jnp.dot(hidden.T, out_grad, preferred_element_type=jnp.float32))
    return (input_grad, gate_mantissa, gate_scales, up_mantissa, up_scales, down_mantissa, down_scales)
```

```python
import jax
import jax.numpy as jnp
import numpy as np
from jax import lax
from jax.sharding import Mesh
from jax.sharding import PartitionSpec as P

PIPE_MODE = "hier"
TENSOR_MODE = "zlo_y"

PIPE = ("z_hi", "x", "core")
TENSOR = ("z_lo", "y")


def quantize_features(grad):
    rows, cols = grad.shape
    blocks = grad.reshape(rows // 32, 32, cols // 2, 2)
    scales = jnp.max(jnp.abs(blocks), axis=(1, 3)) + 1e-06
    mantissa = (blocks / scales[:, None, :, None]).reshape(grad.shape)
    return (mantissa.astype(jnp.bfloat16), scales)


def quantize_hidden(grad):
    rows, cols = grad.shape
    blocks = grad.reshape(rows // 2, 2, cols // 32, 32)
    scales = jnp.max(jnp.abs(blocks), axis=(1, 3)) + 1e-06
    mantissa = (blocks / scales[:, None, :, None]).reshape(grad.shape)
    return (mantissa.astype(jnp.bfloat16), scales)


def contract_last(left, right):
    return lax.dot_general(
        left, right, (((1,), (1,)), ((), ())), preferred_element_type=jnp.float32
    )


def contract_first(left, right):
    return lax.dot_general(
        left, right, (((0,), (0,)), ((), ())), preferred_element_type=jnp.float32
    )


def gate_terms(gate, up, hidden_grad):
    sigmoid_gate = jax.nn.sigmoid(gate)
    silu_gate = gate * sigmoid_gate
    hidden = (silu_gate * up).astype(jnp.bfloat16)
    gate_grad = (hidden_grad * up * sigmoid_gate * (1.0 + gate * (1.0 - sigmoid_gate))).astype(
        jnp.bfloat16
    )
    up_grad = (hidden_grad * silu_gate).astype(jnp.bfloat16)
    return (hidden, gate_grad, up_grad)


def pipe_exchange(parts):
    if PIPE_MODE == "flat_ar":
        gate, up, hidden_grad = lax.psum(tuple(parts), PIPE)
        return gate_terms(gate, up, hidden_grad)
    stacked = jnp.stack(parts)
    if PIPE_MODE == "flat":
        shard = lax.psum_scatter(stacked, PIPE, scatter_dimension=1, tiled=True)
    else:
        shard = stacked
        for axis in ("core", "x", "z_hi"):
            shard = lax.psum_scatter(shard, axis, scatter_dimension=1, tiled=True)
    products = jnp.stack(gate_terms(shard[0], shard[1], shard[2]))
    if PIPE_MODE == "flat":
        full = lax.all_gather(products, PIPE, axis=1, tiled=True)
    else:
        full = products
        for axis in ("z_hi", "x", "core"):
            full = lax.all_gather(full, axis, axis=1, tiled=True)
    return full[0], full[1], full[2]


def tensor_exchange(partial, n_zlo, n_y):
    if TENSOR_MODE == "flat":
        return lax.psum_scatter(partial, TENSOR, scatter_dimension=0, tiled=True)
    if TENSOR_MODE == "zlo_y":
        partial = lax.psum_scatter(partial, "z_lo", scatter_dimension=0, tiled=True)
        return lax.psum_scatter(partial, "y", scatter_dimension=0, tiled=True)
    rows, cols = partial.shape
    blocks = partial.reshape(n_zlo, n_y, rows // (n_zlo * n_y), cols)
    blocks = jnp.swapaxes(blocks, 0, 1).reshape(rows, cols)
    blocks = lax.psum_scatter(blocks, "y", scatter_dimension=0, tiled=True)
    return lax.psum_scatter(blocks, "z_lo", scatter_dimension=0, tiled=True)


def make_on_device(n_zlo, n_y):
    def on_device(tokens, out_grad, w_gate, w_up, w_down):
        gate_part = jnp.dot(tokens, w_gate, preferred_element_type=jnp.float32)
        up_part = jnp.dot(tokens, w_up, preferred_element_type=jnp.float32)
        hidden_part = contract_last(out_grad, w_down)
        hidden, gate_grad, up_grad = pipe_exchange((gate_part, up_part, hidden_part))
        input_grad = tensor_exchange(
            contract_last(gate_grad, w_gate) + contract_last(up_grad, w_up), n_zlo, n_y
        )
        gate_mantissa, gate_scales = quantize_features(contract_first(tokens, gate_grad))
        up_mantissa, up_scales = quantize_features(contract_first(tokens, up_grad))
        down_mantissa, down_scales = quantize_hidden(contract_first(hidden, out_grad))
        return (
            input_grad,
            gate_mantissa,
            gate_scales,
            up_mantissa,
            up_scales,
            down_mantissa,
            down_scales,
        )

    return on_device


def fine_mesh(mesh):
    n_pipe, n_tensor = mesh.shape["pipe"], mesh.shape["tensor"]
    n_y = 4
    n_zlo = n_tensor // n_y
    n_core = 2
    n_x = 4
    n_zhi = n_pipe // (n_core * n_x)
    devices = np.asarray(mesh.devices).reshape(n_zhi, n_x, n_core, n_zlo, n_y)
    return Mesh(devices, ("z_hi", "x", "core", "z_lo", "y")), n_zlo, n_y


def solution(mesh):
    fine, n_zlo, n_y = fine_mesh(mesh)
    in_specs = (
        P(None, PIPE),
        P(None, PIPE),
        P(PIPE, TENSOR),
        P(PIPE, TENSOR),
        P(TENSOR, PIPE),
    )
    out_specs = (
        P(TENSOR, PIPE),
        P(PIPE, TENSOR),
        P(PIPE, TENSOR),
        P(PIPE, TENSOR),
        P(PIPE, TENSOR),
        P(TENSOR, PIPE),
        P(TENSOR, PIPE),
    )
    return jax.shard_map(
        make_on_device(n_zlo, n_y),
        mesh=fine,
        in_specs=in_specs,
        out_specs=out_specs,
        check_vma=False,
    )
```

```python
import jax
import jax.numpy as jnp
import numpy as np
from jax import lax
from jax.sharding import Mesh
from jax.sharding import PartitionSpec as P

PIPE_MODE = "ppermute"
TENSOR_MODE = "ppermute"

FINE = ("z_hi", "x2", "x1", "core", "z4", "z2", "z1", "y2", "y1")
PIPE = ("z_hi", "x2", "x1", "core")
TENSOR = ("z4", "z2", "z1", "y2", "y1")
PIPE_STAGES = ("core", "x1", "x2", "z_hi")
TENSOR_STAGES = ("z1", "z2", "z4", "y1", "y2")


def quantize_features(grad):
    rows, cols = grad.shape
    blocks = grad.reshape(rows // 32, 32, cols // 2, 2)
    scales = jnp.max(jnp.abs(blocks), axis=(1, 3)) + 1e-06
    mantissa = (blocks / scales[:, None, :, None]).reshape(grad.shape)
    return (mantissa.astype(jnp.bfloat16), scales)


def quantize_hidden(grad):
    rows, cols = grad.shape
    blocks = grad.reshape(rows // 2, 2, cols // 32, 32)
    scales = jnp.max(jnp.abs(blocks), axis=(1, 3)) + 1e-06
    mantissa = (blocks / scales[:, None, :, None]).reshape(grad.shape)
    return (mantissa.astype(jnp.bfloat16), scales)


def contract_last(left, right):
    return lax.dot_general(
        left, right, (((1,), (1,)), ((), ())), preferred_element_type=jnp.float32
    )


def contract_first(left, right):
    return lax.dot_general(
        left, right, (((0,), (0,)), ((), ())), preferred_element_type=jnp.float32
    )


def gate_terms(gate, up, hidden_grad):
    sigmoid_gate = jax.nn.sigmoid(gate)
    silu_gate = gate * sigmoid_gate
    hidden = (silu_gate * up).astype(jnp.bfloat16)
    gate_grad = (hidden_grad * up * sigmoid_gate * (1.0 + gate * (1.0 - sigmoid_gate))).astype(
        jnp.bfloat16
    )
    up_grad = (hidden_grad * silu_gate).astype(jnp.bfloat16)
    return (hidden, gate_grad, up_grad)


def halve(x, axis, dim, mode):
    if mode == "xla":
        return lax.psum_scatter(x, axis, scatter_dimension=dim, tiled=True)
    half = x.shape[dim] // 2
    me = lax.axis_index(axis)
    keep = lax.dynamic_slice_in_dim(x, me * half, half, axis=dim)
    send = lax.dynamic_slice_in_dim(x, (1 - me) * half, half, axis=dim)
    return keep + lax.ppermute(send, axis, perm=[(0, 1), (1, 0)])


def double(x, axis, dim, mode):
    if mode == "xla":
        return lax.all_gather(x, axis, axis=dim, tiled=True)
    me = lax.axis_index(axis)
    other = lax.ppermute(x, axis, perm=[(0, 1), (1, 0)])
    both = jnp.concatenate([other, other], axis=dim)
    return lax.dynamic_update_slice_in_dim(both, x, me * x.shape[dim], axis=dim)


def pipe_exchange(parts):
    shard = jnp.stack(parts)
    for axis in PIPE_STAGES:
        shard = halve(shard, axis, 1, PIPE_MODE)
    full = jnp.stack(gate_terms(shard[0], shard[1], shard[2]))
    for axis in reversed(PIPE_STAGES):
        full = double(full, axis, 1, PIPE_MODE)
    return full[0], full[1], full[2]


def tensor_exchange(partial):
    rows, cols = partial.shape
    bits = len(TENSOR)
    blocks = partial.reshape((2,) * bits + (rows >> bits, cols))
    order = [TENSOR.index(a) for a in TENSOR_STAGES]
    blocks = jnp.transpose(blocks, order + [bits, bits + 1]).reshape(rows, cols)
    for axis in TENSOR_STAGES:
        blocks = halve(blocks, axis, 0, TENSOR_MODE)
    return blocks


def make_on_device():
    def on_device(tokens, out_grad, w_gate, w_up, w_down):
        gate_part = jnp.dot(tokens, w_gate, preferred_element_type=jnp.float32)
        up_part = jnp.dot(tokens, w_up, preferred_element_type=jnp.float32)
        hidden_part = contract_last(out_grad, w_down)
        hidden, gate_grad, up_grad = pipe_exchange((gate_part, up_part, hidden_part))
        input_grad = tensor_exchange(
            contract_last(gate_grad, w_gate) + contract_last(up_grad, w_up)
        )
        gate_mantissa, gate_scales = quantize_features(contract_first(tokens, gate_grad))
        up_mantissa, up_scales = quantize_features(contract_first(tokens, up_grad))
        down_mantissa, down_scales = quantize_hidden(contract_first(hidden, out_grad))
        return (
            input_grad,
            gate_mantissa,
            gate_scales,
            up_mantissa,
            up_scales,
            down_mantissa,
            down_scales,
        )

    return on_device


def fine_mesh(mesh):
    n_pipe, n_tensor = mesh.shape["pipe"], mesh.shape["tensor"]
    assert n_pipe == 16 and n_tensor == 32
    devices = np.asarray(mesh.devices).reshape((2,) * len(FINE))
    return Mesh(devices, FINE)


def solution(mesh):
    fine = fine_mesh(mesh)
    in_specs = (
        P(None, PIPE),
        P(None, PIPE),
        P(PIPE, TENSOR),
        P(PIPE, TENSOR),
        P(TENSOR, PIPE),
    )
    out_specs = (
        P(TENSOR, PIPE),
        P(PIPE, TENSOR),
        P(PIPE, TENSOR),
        P(PIPE, TENSOR),
        P(PIPE, TENSOR),
        P(TENSOR, PIPE),
        P(TENSOR, PIPE),
    )
    return jax.shard_map(
        make_on_device(),
        mesh=fine,
        in_specs=in_specs,
        out_specs=out_specs,
        check_vma=False,
    )
```

```python
import jax
import jax.numpy as jnp
import numpy as np
from jax import lax
from jax.sharding import Mesh
from jax.sharding import PartitionSpec as P

X_MODE = "direct"
Y_MODE = "direct"

if X_MODE == "direct":
    PIPE = ("z_hi", "x", "core")
    PIPE_STAGES = ("core", "x", "z_hi")
else:
    PIPE = ("z_hi", "x2", "x1", "core")
    PIPE_STAGES = ("core", "x1", "x2", "z_hi")
if Y_MODE == "direct":
    TENSOR = ("z4", "z2", "z1", "y")
    TENSOR_STAGES = ("y", "z1", "z2", "z4")
else:
    TENSOR = ("z4", "z2", "z1", "y2", "y1")
    TENSOR_STAGES = ("z1", "z2", "z4", "y1", "y2")
FINE = PIPE + TENSOR


def quantize_features(grad):
    rows, cols = grad.shape
    blocks = grad.reshape(rows // 32, 32, cols // 2, 2)
    scales = jnp.max(jnp.abs(blocks), axis=(1, 3)) + 1e-06
    mantissa = (blocks / scales[:, None, :, None]).reshape(grad.shape)
    return (mantissa.astype(jnp.bfloat16), scales)


def quantize_hidden(grad):
    rows, cols = grad.shape
    blocks = grad.reshape(rows // 2, 2, cols // 32, 32)
    scales = jnp.max(jnp.abs(blocks), axis=(1, 3)) + 1e-06
    mantissa = (blocks / scales[:, None, :, None]).reshape(grad.shape)
    return (mantissa.astype(jnp.bfloat16), scales)


def contract_last(left, right):
    return lax.dot_general(
        left, right, (((1,), (1,)), ((), ())), preferred_element_type=jnp.float32
    )


def contract_first(left, right):
    return lax.dot_general(
        left, right, (((0,), (0,)), ((), ())), preferred_element_type=jnp.float32
    )


def gate_terms(gate, up, hidden_grad):
    sigmoid_gate = jax.nn.sigmoid(gate)
    silu_gate = gate * sigmoid_gate
    hidden = (silu_gate * up).astype(jnp.bfloat16)
    gate_grad = (hidden_grad * up * sigmoid_gate * (1.0 + gate * (1.0 - sigmoid_gate))).astype(
        jnp.bfloat16
    )
    up_grad = (hidden_grad * silu_gate).astype(jnp.bfloat16)
    return (hidden, gate_grad, up_grad)


def scatter_sum(x, axis, dim):
    n = lax.psum(1, axis)
    size = x.shape[dim] // n
    me = lax.axis_index(axis)
    acc = lax.dynamic_slice_in_dim(x, me * size, size, axis=dim)
    for shift in range(1, n):
        send = lax.dynamic_slice_in_dim(x, ((me + shift) % n) * size, size, axis=dim)
        perm = [(j, (j + shift) % n) for j in range(n)]
        acc = acc + lax.ppermute(send, axis, perm=perm)
    return acc


def gather(x, axis, dim):
    n = lax.psum(1, axis)
    size = x.shape[dim]
    me = lax.axis_index(axis)
    full = jnp.concatenate([x] * n, axis=dim)
    for shift in range(1, n):
        perm = [(j, (j + shift) % n) for j in range(n)]
        got = lax.ppermute(x, axis, perm=perm)
        full = lax.dynamic_update_slice_in_dim(full, got, ((me - shift) % n) * size, axis=dim)
    return full


def pipe_exchange(parts):
    shard = jnp.stack(parts)
    for axis in PIPE_STAGES:
        shard = scatter_sum(shard, axis, 1)
    full = jnp.stack(gate_terms(shard[0], shard[1], shard[2]))
    for axis in reversed(PIPE_STAGES):
        full = gather(full, axis, 1)
    return full[0], full[1], full[2]


def tensor_exchange(partial, sizes):
    rows, cols = partial.shape
    count = len(TENSOR)
    blocks = partial.reshape(tuple(sizes[a] for a in TENSOR) + (-1, cols))
    order = [TENSOR.index(a) for a in TENSOR_STAGES]
    blocks = jnp.transpose(blocks, order + [count, count + 1]).reshape(rows, cols)
    for axis in TENSOR_STAGES:
        blocks = scatter_sum(blocks, axis, 0)
    return blocks


def make_on_device(sizes):
    def on_device(tokens, out_grad, w_gate, w_up, w_down):
        gate_part = jnp.dot(tokens, w_gate, preferred_element_type=jnp.float32)
        up_part = jnp.dot(tokens, w_up, preferred_element_type=jnp.float32)
        hidden_part = contract_last(out_grad, w_down)
        hidden, gate_grad, up_grad = pipe_exchange((gate_part, up_part, hidden_part))
        input_grad = tensor_exchange(
            contract_last(gate_grad, w_gate) + contract_last(up_grad, w_up), sizes
        )
        gate_mantissa, gate_scales = quantize_features(contract_first(tokens, gate_grad))
        up_mantissa, up_scales = quantize_features(contract_first(tokens, up_grad))
        down_mantissa, down_scales = quantize_hidden(contract_first(hidden, out_grad))
        return (
            input_grad,
            gate_mantissa,
            gate_scales,
            up_mantissa,
            up_scales,
            down_mantissa,
            down_scales,
        )

    return on_device


def fine_mesh(mesh):
    n_pipe, n_tensor = mesh.shape["pipe"], mesh.shape["tensor"]
    assert n_pipe == 16 and n_tensor == 32
    sizes = {"z_hi": 2, "x": 4, "core": 2, "y": 4}
    for axis in FINE:
        sizes.setdefault(axis, 2)
    devices = np.asarray(mesh.devices).reshape(tuple(sizes[a] for a in FINE))
    return Mesh(devices, FINE), sizes


def solution(mesh):
    fine, sizes = fine_mesh(mesh)
    in_specs = (
        P(None, PIPE),
        P(None, PIPE),
        P(PIPE, TENSOR),
        P(PIPE, TENSOR),
        P(TENSOR, PIPE),
    )
    out_specs = (
        P(TENSOR, PIPE),
        P(PIPE, TENSOR),
        P(PIPE, TENSOR),
        P(PIPE, TENSOR),
        P(PIPE, TENSOR),
        P(TENSOR, PIPE),
        P(TENSOR, PIPE),
    )
    return jax.shard_map(
        make_on_device(sizes),
        mesh=fine,
        in_specs=in_specs,
        out_specs=out_specs,
        check_vma=False,
    )
```

```python
import jax
import jax.numpy as jnp
import numpy as np
from jax import lax
from jax.sharding import Mesh
from jax.sharding import PartitionSpec as P

X_MODE = "direct"
Y_MODE = "direct"

if X_MODE == "direct":
    PIPE = ("z_hi", "x", "core")
    PIPE_STAGES = ("core", "x", "z_hi")
else:
    PIPE = ("z_hi", "x2", "x1", "core")
    PIPE_STAGES = ("core", "x1", "x2", "z_hi")
if Y_MODE == "direct":
    TENSOR = ("z4", "z2", "z1", "y")
    TENSOR_STAGES = ("y", "z1", "z2", "z4")
else:
    TENSOR = ("z4", "z2", "z1", "y2", "y1")
    TENSOR_STAGES = ("z1", "z2", "z4", "y1", "y2")
FINE = PIPE + TENSOR


def quantize_features(grad):
    rows, cols = grad.shape
    blocks = grad.reshape(rows // 32, 32, cols // 2, 2)
    scales = jnp.max(jnp.abs(blocks), axis=(1, 3)) + 1e-06
    mantissa = (blocks / scales[:, None, :, None]).reshape(grad.shape)
    return (mantissa.astype(jnp.bfloat16), scales)


def quantize_hidden(grad):
    rows, cols = grad.shape
    blocks = grad.reshape(rows // 2, 2, cols // 32, 32)
    scales = jnp.max(jnp.abs(blocks), axis=(1, 3)) + 1e-06
    mantissa = (blocks / scales[:, None, :, None]).reshape(grad.shape)
    return (mantissa.astype(jnp.bfloat16), scales)


def transposed(pair):
    return (pair[0].T, pair[1].T)


def contract_last(left, right):
    return lax.dot_general(
        left, right, (((1,), (1,)), ((), ())), preferred_element_type=jnp.float32
    )


def contract_first(left, right):
    return lax.dot_general(
        left, right, (((0,), (0,)), ((), ())), preferred_element_type=jnp.float32
    )


def gate_terms(gate, up, hidden_grad):
    sigmoid_gate = jax.nn.sigmoid(gate)
    silu_gate = gate * sigmoid_gate
    hidden = (silu_gate * up).astype(jnp.bfloat16)
    gate_grad = (hidden_grad * up * sigmoid_gate * (1.0 + gate * (1.0 - sigmoid_gate))).astype(
        jnp.bfloat16
    )
    up_grad = (hidden_grad * silu_gate).astype(jnp.bfloat16)
    return (hidden, gate_grad, up_grad)


def scatter_sum(x, axis, dim):
    n = lax.psum(1, axis)
    size = x.shape[dim] // n
    me = lax.axis_index(axis)
    acc = lax.dynamic_slice_in_dim(x, me * size, size, axis=dim)
    for shift in range(1, n):
        send = lax.dynamic_slice_in_dim(x, ((me + shift) % n) * size, size, axis=dim)
        perm = [(j, (j + shift) % n) for j in range(n)]
        acc = acc + lax.ppermute(send, axis, perm=perm)
    return acc


def gather(x, axis, dim):
    n = lax.psum(1, axis)
    size = x.shape[dim]
    me = lax.axis_index(axis)
    full = jnp.concatenate([x] * n, axis=dim)
    for shift in range(1, n):
        perm = [(j, (j + shift) % n) for j in range(n)]
        got = lax.ppermute(x, axis, perm=perm)
        full = lax.dynamic_update_slice_in_dim(full, got, ((me - shift) % n) * size, axis=dim)
    return full


def pipe_exchange(parts):
    shard = jnp.stack(parts)
    for axis in PIPE_STAGES:
        shard = scatter_sum(shard, axis, 1)
    full = jnp.stack(gate_terms(shard[0], shard[1], shard[2]))
    for axis in reversed(PIPE_STAGES):
        full = gather(full, axis, 1)
    return full[0], full[1], full[2]


def tensor_exchange(partial, sizes):
    rows, cols = partial.shape
    count = len(TENSOR)
    blocks = partial.reshape(tuple(sizes[a] for a in TENSOR) + (-1, cols))
    order = [TENSOR.index(a) for a in TENSOR_STAGES]
    blocks = jnp.transpose(blocks, order + [count, count + 1]).reshape(rows, cols)
    for axis in TENSOR_STAGES:
        blocks = scatter_sum(blocks, axis, 0)
    return blocks


def make_on_device(sizes):
    def on_device(tokens, out_grad, w_gate, w_up, w_down):
        gate_part = jnp.dot(tokens, w_gate, preferred_element_type=jnp.float32)
        up_part = jnp.dot(tokens, w_up, preferred_element_type=jnp.float32)
        hidden_part = contract_last(out_grad, w_down)
        hidden, gate_grad, up_grad = pipe_exchange((gate_part, up_part, hidden_part))
        input_grad = tensor_exchange(
            contract_last(gate_grad, w_gate) + contract_last(up_grad, w_up), sizes
        )
        gate_mantissa, gate_scales = transposed(quantize_hidden(contract_first(gate_grad, tokens)))
        up_mantissa, up_scales = transposed(quantize_hidden(contract_first(up_grad, tokens)))
        down_mantissa, down_scales = quantize_hidden(contract_first(hidden, out_grad))
        return (
            input_grad,
            gate_mantissa,
            gate_scales,
            up_mantissa,
            up_scales,
            down_mantissa,
            down_scales,
        )

    return on_device


def fine_mesh(mesh):
    n_pipe, n_tensor = mesh.shape["pipe"], mesh.shape["tensor"]
    assert n_pipe == 16 and n_tensor == 32
    sizes = {"z_hi": 2, "x": 4, "core": 2, "y": 4}
    for axis in FINE:
        sizes.setdefault(axis, 2)
    devices = np.asarray(mesh.devices).reshape(tuple(sizes[a] for a in FINE))
    return Mesh(devices, FINE), sizes


def solution(mesh):
    fine, sizes = fine_mesh(mesh)
    in_specs = (
        P(None, PIPE),
        P(None, PIPE),
        P(PIPE, TENSOR),
        P(PIPE, TENSOR),
        P(TENSOR, PIPE),
    )
    out_specs = (
        P(TENSOR, PIPE),
        P(PIPE, TENSOR),
        P(PIPE, TENSOR),
        P(PIPE, TENSOR),
        P(PIPE, TENSOR),
        P(TENSOR, PIPE),
        P(TENSOR, PIPE),
    )
    return jax.shard_map(
        make_on_device(sizes),
        mesh=fine,
        in_specs=in_specs,
        out_specs=out_specs,
        check_vma=False,
    )
```

```python
import jax
import jax.numpy as jnp
import numpy as np
from jax import lax
from jax.sharding import Mesh
from jax.sharding import PartitionSpec as P

X_MODE = "direct"
Y_MODE = "direct"

if X_MODE == "direct":
    PIPE = ("z_hi", "x", "core")
    PIPE_STAGES = ("core", "x", "z_hi")
else:
    PIPE = ("z_hi", "x2", "x1", "core")
    PIPE_STAGES = ("core", "x1", "x2", "z_hi")
if Y_MODE == "direct":
    TENSOR = ("z4", "z2", "z1", "y")
    TENSOR_STAGES = ("y", "z1", "z2", "z4")
else:
    TENSOR = ("z4", "z2", "z1", "y2", "y1")
    TENSOR_STAGES = ("z1", "z2", "z4", "y1", "y2")
FINE = PIPE + TENSOR


def quantize_hidden(grad):
    rows, cols = grad.shape
    blocks = grad.reshape(rows // 2, 2, cols // 32, 32)
    scales = jnp.max(jnp.abs(blocks), axis=(1, 3)) + 1e-06
    mantissa = (blocks / scales[:, None, :, None]).reshape(grad.shape)
    return (mantissa.astype(jnp.bfloat16), scales)


def transposed(pair):
    return (pair[0].T, pair[1].T)


def contract_last(left, right):
    return lax.dot_general(
        left, right, (((1,), (1,)), ((), ())), preferred_element_type=jnp.float32
    )


def contract_first(left, right):
    return lax.dot_general(
        left, right, (((0,), (0,)), ((), ())), preferred_element_type=jnp.float32
    )


def gate_terms(gate, up, hidden_grad):
    sigmoid_gate = jax.nn.sigmoid(gate)
    silu_gate = gate * sigmoid_gate
    hidden = (silu_gate * up).astype(jnp.bfloat16)
    gate_grad = (hidden_grad * up * sigmoid_gate * (1.0 + gate * (1.0 - sigmoid_gate))).astype(
        jnp.bfloat16
    )
    up_grad = (hidden_grad * silu_gate).astype(jnp.bfloat16)
    return (hidden, gate_grad, up_grad)


def scatter_sum(x, axis, dim):
    n = lax.psum(1, axis)
    size = x.shape[dim] // n
    me = lax.axis_index(axis)
    acc = lax.dynamic_slice_in_dim(x, me * size, size, axis=dim)
    for shift in range(1, n):
        send = lax.dynamic_slice_in_dim(x, ((me + shift) % n) * size, size, axis=dim)
        perm = [(j, (j + shift) % n) for j in range(n)]
        acc = acc + lax.ppermute(send, axis, perm=perm)
    return acc


def gather(x, axis, dim):
    n = lax.psum(1, axis)
    size = x.shape[dim]
    me = lax.axis_index(axis)
    full = jnp.concatenate([x] * n, axis=dim)
    for shift in range(1, n):
        perm = [(j, (j + shift) % n) for j in range(n)]
        got = lax.ppermute(x, axis, perm=perm)
        full = lax.dynamic_update_slice_in_dim(full, got, ((me - shift) % n) * size, axis=dim)
    return full


def pipe_exchange(parts):
    shard = jnp.stack(parts)
    for axis in PIPE_STAGES:
        shard = scatter_sum(shard, axis, 1)
    full = jnp.stack(gate_terms(shard[0], shard[1], shard[2]))
    for axis in reversed(PIPE_STAGES):
        full = gather(full, axis, 1)
    return full[0], full[1], full[2]


def tensor_exchange(partial, sizes):
    rows, cols = partial.shape
    count = len(TENSOR)
    blocks = partial.reshape(tuple(sizes[a] for a in TENSOR) + (-1, cols))
    order = [TENSOR.index(a) for a in TENSOR_STAGES]
    blocks = jnp.transpose(blocks, order + [count, count + 1]).reshape(rows, cols)
    for axis in TENSOR_STAGES:
        blocks = scatter_sum(blocks, axis, 0)
    return blocks


def make_on_device(sizes):
    def body(tokens, out_grad, w_gate, w_up, w_down):
        gate_part = jnp.dot(tokens, w_gate, preferred_element_type=jnp.float32)
        up_part = jnp.dot(tokens, w_up, preferred_element_type=jnp.float32)
        hidden_part = contract_last(out_grad, w_down)
        hidden, gate_grad, up_grad = pipe_exchange((gate_part, up_part, hidden_part))
        input_grad = tensor_exchange(
            contract_last(gate_grad, w_gate) + contract_last(up_grad, w_up), sizes
        )
        gate_mantissa, gate_scales = transposed(quantize_hidden(contract_first(gate_grad, tokens)))
        up_mantissa, up_scales = transposed(quantize_hidden(contract_first(up_grad, tokens)))
        down_mantissa, down_scales = quantize_hidden(contract_first(hidden, out_grad))
        return (
            input_grad,
            gate_mantissa,
            gate_scales,
            up_mantissa,
            up_scales,
            down_mantissa,
            down_scales,
        )

    return body


def fine_mesh(mesh):
    n_pipe, n_tensor = mesh.shape["pipe"], mesh.shape["tensor"]
    assert n_pipe == 16 and n_tensor == 32
    sizes = {"z_hi": 2, "x": 4, "core": 2, "y": 4}
    for axis in FINE:
        sizes.setdefault(axis, 2)
    devices = np.asarray(mesh.devices).reshape(tuple(sizes[a] for a in FINE))
    return Mesh(devices, FINE), sizes


def solution(mesh):
    fine, sizes = fine_mesh(mesh)
    in_specs = (
        P(None, PIPE),
        P(None, PIPE),
        P(PIPE, TENSOR),
        P(PIPE, TENSOR),
        P(TENSOR, PIPE),
    )
    out_specs = (
        P(TENSOR, PIPE),
        P(PIPE, TENSOR),
        P(PIPE, TENSOR),
        P(PIPE, TENSOR),
        P(PIPE, TENSOR),
        P(TENSOR, PIPE),
        P(TENSOR, PIPE),
    )
    return jax.shard_map(
        make_on_device(sizes),
        mesh=fine,
        in_specs=in_specs,
        out_specs=out_specs,
        check_vma=False,
    )
```
